512 devices in a mesh: row: 32 (over z_lo, y), col: 16 (over z_hi, x, core).
Axes of the slice: x: 4, y: 4, z: 16 (z_hi: 2, z_lo: 8; z = z_hi * 8 + z_lo), core: 2. Of those that a mesh axis runs over, the one named last changes fastest.
Arguments:
- rhs: bfloat16 [32, 16, 64, 768], P('row', 'col'), may hold values from -6 to 6
- operator_blocks: bfloat16 [32, 16, 768, 768], P('row', 'col'), may hold values from -0.5 to 3.5
- local_solver: bfloat16 [32, 16, 768, 768], P('row', 'col'), may hold values from -0.1 to 0.6
- modes: bfloat16 [32, 16, 48, 768], P('row', 'col'), may hold values from -0.21875 to 0.21875
- coupling: bfloat16 [32, 16, 4, 128, 128], P('row', 'col'), may hold values from -0.25 to 0.25
- coarse_inverse: bfloat16 [16, 1536, 32, 768], P('col', None, 'row'), may hold values from -0.05 to 0.15
- send_block: int32 [32, 16, 8], P('row', 'col'), may hold values from 0 to 5
- slot_dir: int32 [32, 16, 4], P('row', 'col'), may hold values from -1 to 7, as said below
- slot_block: int32 [32, 16, 4], P('row', 'col'), may hold values from 0 to 5
Outputs:
- solution: float32 [32, 16, 64, 768], P('row', 'col')
The draws below stay inside these ranges and needn't reach their ends.
Inputs may be any that keep to these rules, and one draw needn't show every extreme that they name: `slot_dir`: each subdomain lists 2 to 4 distinct directions toward subdomains inside the grid in its first slots; the remaining slots hold -1.
All inputs are finite; a program needn't handle non-finite values.
Results may differ from the reference program's by a relative error of at most 0.0033.
Values may be sent and summed in bfloat16 or wider, within the bound.
No kernel may reach another device: no remote copies, remote signals or barrier semaphores. Data moves between devices by JAX's collectives and lax.ppermute only.
A program may use at most 64 MiB of HBM per device.

```python
import jax
import jax.numpy as jnp
from jax import lax

SUB = 768
BLK = 128
NBLK = 6
MODES = 48
COLS = 64
SLOTS = 4
NDIR = 8
ITERS = 6
GRID_ROWS = 32
GRID_COLS = 16


def diagonal_values(key):
    uniform_part = jax.random.uniform(jax.random.fold_in(key, 21), (GRID_ROWS, GRID_COLS, SUB), jnp.float32, 0.0, 1.0)
    return jnp.exp(uniform_part * jnp.log(3.0))


def identity_mask():
    return (jnp.arange(SUB)[:, None] == jnp.arange(SUB)[None, :]).astype(jnp.float32)


def draw_operator_blocks(key, part):
    diagonal = diagonal_values(key)
    shape = (GRID_ROWS, GRID_COLS, SUB, SUB)
    noise = jax.random.normal(jax.random.fold_in(key, 22), shape, jnp.float32) * 0.015
    return (noise + identity_mask() * diagonal[..., :, None]).astype(jnp.bfloat16)


def draw_local_solver(key, part):
    diagonal = diagonal_values(key)
    shape = (GRID_ROWS, GRID_COLS, SUB, SUB)
    noise = jax.random.normal(jax.random.fold_in(key, 23), shape, jnp.float32) * 0.0025
    return (noise + identity_mask() * (0.5 / diagonal)[..., :, None]).astype(jnp.bfloat16)


def draw_coarse_inverse(key, part):
    shape = (GRID_COLS, GRID_ROWS * MODES, GRID_ROWS, GRID_COLS * MODES)
    col_in = jnp.arange(GRID_COLS)[:, None, None, None]
    row_in = (jnp.arange(GRID_ROWS * MODES) // MODES)[None, :, None, None]
    mode_in = (jnp.arange(GRID_ROWS * MODES) % MODES)[None, :, None, None]
    row_out = jnp.arange(GRID_ROWS)[None, None, :, None]
    col_out = (jnp.arange(GRID_COLS * MODES) // MODES)[None, None, None, :]
    mode_out = (jnp.arange(GRID_COLS * MODES) % MODES)[None, None, None, :]
    aligned = (row_in == row_out) & (mode_in == mode_out)
    same = aligned & (col_in == col_out)
    after = aligned & (col_in == (col_out + 1) % GRID_COLS)
    before = aligned & (col_in == (col_out + GRID_COLS - 1) % GRID_COLS)
    noise = jax.random.normal(jax.random.fold_in(key, 31), shape, jnp.float32) * 0.0025
    structured = same.astype(jnp.float32) * 0.1 + (after | before).astype(jnp.float32) * 0.08
    return (noise + structured).astype(jnp.bfloat16)


def draw_slot_dir(key, part):
    rows = jnp.arange(GRID_ROWS)[:, None, None]
    cols = jnp.arange(GRID_COLS)[None, :, None]
    offset_a = jnp.array([-1, -1, -1, 0, 0, 1, 1, 1], jnp.int32)[None, None, :]
    offset_b = jnp.array([-1, 0, 1, -1, 1, -1, 0, 1], jnp.int32)[None, None, :]
    valid = (rows + offset_a >= 0) & (rows + offset_a < GRID_ROWS) & (cols + offset_b >= 0) & (cols + offset_b < GRID_COLS)
    scores = jax.random.randint(jax.random.fold_in(key, 41), (GRID_ROWS, GRID_COLS, NDIR), 0, 1 << 20) * NDIR + jnp.arange(NDIR)
    scores = jnp.where(valid, scores, -1)
    order = jnp.argsort(-scores, axis=-1, stable=True).astype(jnp.int32)
    valid_count = jnp.sum(valid.astype(jnp.int32), axis=-1)
    listed = jax.random.randint(jax.random.fold_in(key, 42), (GRID_ROWS, GRID_COLS), 2, SLOTS + 1)
    forced = (jnp.arange(GRID_ROWS)[:, None] + jnp.arange(GRID_COLS)[None, :]) % 3 == 0
    listed = jnp.where(forced, SLOTS, listed)
    listed = jnp.minimum(listed, valid_count)
    taken = order[..., :SLOTS]
    return jnp.where(jnp.arange(SLOTS)[None, None, :] < listed[..., None], taken, -1).astype(jnp.int32)


def place_ends(values, own_key, smallest, top_value):
    index_at = [jax.random.randint(jax.random.fold_in(own_key, axis), (), 0, length) for axis, length in enumerate(values.shape)]
    longest = values.shape.index(max(values.shape))
    beside = index_at[:longest] + [(index_at[longest] + 1) % values.shape[longest]] + index_at[longest + 1:]
    return values.at[tuple(index_at)].set(smallest).at[tuple(beside)].set(top_value)


def block_scale(key, shape, split, smallest, largest):
    def one(position, shards_of):
        steps = jax.random.uniform(jax.random.fold_in(jax.random.fold_in(key, 6), position), (shards_of,), jnp.float32, smallest / len(split), largest / len(split))
        return jnp.repeat(jnp.exp(steps), shape[position] // shards_of).reshape((-1,) + (1,) * (len(shape) - position - 1))

    loudness = one(*split[0])
    for cut in split[1:]:
        loudness = loudness * one(*cut)
    return loudness


def gaussian(key, dims, width, bound, pieces=(), held_as=jnp.bfloat16):
    gain = block_scale(key, dims, pieces, -0.22, 0.18) if pieces else 1.0
    values = jax.random.normal(key, dims, jnp.float32) * width * gain
    return jnp.minimum(jnp.maximum(values, -bound), bound).astype(held_as)


def setup_inputs(seed: int = 0) -> dict:
    splits = jax.random.split(jax.random.key(seed), 10)
    return {
        "rhs": gaussian(splits[0], (GRID_ROWS, GRID_COLS, COLS, SUB), 1.0, 6.0, ((0, 32), (1, 16))),
        "operator_blocks": draw_operator_blocks(jax.random.fold_in(splits[9], 71), 0),
        "local_solver": draw_local_solver(jax.random.fold_in(splits[9], 71), 0),
        "modes": gaussian(splits[3], (GRID_ROWS, GRID_COLS, MODES, SUB), SUB ** -0.5, 0.21875, ((0, 32), (1, 16))),
        "coupling": gaussian(splits[4], (GRID_ROWS, GRID_COLS, SLOTS, BLK, BLK), (4 * BLK) ** -0.5, 0.25, ((0, 32), (1, 16))),
        "coarse_inverse": draw_coarse_inverse(jax.random.fold_in(splits[9], 71), 0),
        "send_block": place_ends(jax.random.randint(splits[6], (GRID_ROWS, GRID_COLS, NDIR), 0, NBLK), jax.random.fold_in(splits[6], 1), 0, NBLK - 1).astype(jnp.int32),
        "slot_dir": draw_slot_dir(jax.random.fold_in(splits[9], 71), 0),
        "slot_block": place_ends(jax.random.randint(splits[8], (GRID_ROWS, GRID_COLS, SLOTS), 0, NBLK), jax.random.fold_in(splits[8], 1), 0, NBLK - 1).astype(jnp.int32),
    }


OFFSETS = ((-1, -1), (-1, 0), (-1, 1), (0, -1), (0, 1), (1, -1), (1, 0), (1, 1))


def reference(rhs, operator_blocks, local_solver, modes, coupling, coarse_inverse, send_block, slot_dir, slot_block):
    highest = lax.Precision.HIGHEST
    subdomains = GRID_ROWS * GRID_COLS
    rhs_full = rhs.astype(jnp.float32)
    flat_operator = operator_blocks.reshape(subdomains, SUB, SUB)
    flat_solver = local_solver.reshape(subdomains, SUB, SUB)
    send_onehot = (send_block[..., None] == jnp.arange(NBLK)).astype(jnp.float32)
    dir_onehot = (slot_dir[..., None] == jnp.arange(NDIR)).astype(jnp.float32)
    block_onehot = (slot_block[..., None] == jnp.arange(NBLK)).astype(jnp.float32)
    coupling_full = coupling.astype(jnp.float32)
    modes_full = modes.astype(jnp.float32)

    def local_product(field_half, matrices):
        def one_block(pair):
            return jnp.dot(pair[0], pair[1], preferred_element_type=jnp.float32)
        result = lax.map(one_block, (field_half.reshape(subdomains, COLS, SUB), matrices))
        return result.reshape(GRID_ROWS, GRID_COLS, COLS, SUB)

    def apply_operator(field_half):
        blocks = field_half.astype(jnp.float32).reshape(GRID_ROWS, GRID_COLS, COLS, NBLK, BLK)
        outgoing = jnp.einsum("abckn,abek->abecn", blocks, send_onehot, precision=highest)
        padded = jnp.pad(outgoing, ((1, 1), (1, 1), (0, 0), (0, 0), (0, 0)))
        arrived = []
        for direction in range(NDIR):
            shift_a, shift_b = OFFSETS[direction]
            arrived.append(padded[1 + shift_a:1 + shift_a + GRID_ROWS, 1 + shift_b:1 + shift_b + GRID_COLS, NDIR - 1 - direction])
        incoming = jnp.stack(arrived, axis=2)
        chosen = jnp.einsum("absd,abdcn->abscn", dir_onehot, incoming, precision=highest)
        coupled = jnp.einsum("abscn,absnm->abscm", chosen, coupling_full, precision=highest)
        placed = jnp.einsum("abscm,absk->abckm", coupled, block_onehot, precision=highest)
        return local_product(field_half, flat_operator) + placed.reshape(GRID_ROWS, GRID_COLS, COLS, SUB)

    def coarse_solve(rounded):
        restricted = jnp.einsum("abms,abcs->abmc", modes_full, rounded.astype(jnp.float32), precision=highest)
        restricted = restricted.astype(jnp.bfloat16)
        inputs = jnp.transpose(restricted, (1, 0, 2, 3)).reshape(GRID_COLS, GRID_ROWS * MODES, COLS)

        def accumulate(total, pair):
            vector, slab = pair
            product = lax.dot_general(vector, slab.reshape(GRID_ROWS * MODES, GRID_ROWS * GRID_COLS * MODES), (((0,), (0,)), ((), ())), preferred_element_type=jnp.float32)
            return total + product, None

        start_total = jnp.zeros((COLS, GRID_ROWS * GRID_COLS * MODES), jnp.float32)
        total, unused = lax.scan(accumulate, start_total, (inputs, coarse_inverse))
        total = jnp.transpose(total.reshape(COLS, GRID_ROWS, GRID_COLS, MODES), (1, 2, 3, 0))
        return total.astype(jnp.bfloat16)

    def prolong(coarse_half):
        return jnp.einsum("abmc,abms->abcs", coarse_half.astype(jnp.float32), modes_full, precision=highest)

    solution = jnp.zeros((GRID_ROWS, GRID_COLS, COLS, SUB), jnp.float32)
    pending = None
    for iteration in range(ITERS):
        if iteration == 0:
            residual = rhs_full
        else:
            residual = rhs_full - apply_operator(solution.astype(jnp.bfloat16))
        rounded = residual.astype(jnp.bfloat16)
        update = local_product(rounded, flat_solver)
        fresh = None
        if iteration + 1 < ITERS:
            fresh = coarse_solve(rounded)
        if pending is not None:
            update = update + prolong(pending)
        solution = solution + update
        pending = fresh
    return solution
```

```python
import jax
import jax.numpy as jnp
from jax import lax
from jax.sharding import PartitionSpec as P

ITERS = 6


OFFSETS = ((-1, -1), (-1, 0), (-1, 1), (0, -1), (0, 1), (1, -1), (1, 0), (1, 1))


def neighbour_pieces(outgoing):
    rows = lax.axis_size("row")
    cols = lax.axis_size("col")
    arrived = []
    for direction in range(8):
        shift_a, shift_b = OFFSETS[direction]
        portion = outgoing[7 - direction]
        route = []
        for a in range(rows):
            for b in range(cols):
                src_a, src_b = a + shift_a, b + shift_b
                if 0 <= src_a < rows and 0 <= src_b < cols:
                    route.append((src_a * cols + src_b, a * cols + b))
        if shift_a == 0:
            route = [(s % cols, t % cols) for s, t in route if s // cols == 0]
            arrived.append(lax.ppermute(portion, "col", route))
        elif shift_b == 0:
            route = [(s // cols, t // cols) for s, t in route if s % cols == 0]
            arrived.append(lax.ppermute(portion, "row", route))
        else:
            arrived.append(lax.ppermute(portion, ("row", "col"), route))
    return jnp.stack(arrived, 0)


def gather_rows(piece, bits):
    index = lax.axis_index("row")
    size = lax.axis_size("row")
    current = piece
    for step, bit in enumerate(bits):
        distance = 1 << bit
        route = [(i, i ^ distance) for i in range(size)]
        other = lax.ppermute(current, "row", route)
        high = ((index >> bit) & 1) == 1
        low_part = jnp.where(high, other, current)
        high_part = jnp.where(high, current, other)
        current = jnp.stack([low_part, high_part], axis=step)
    return current


def scatter_cols(partial, bits):
    index = lax.axis_index("col")
    size = lax.axis_size("col")
    total_bits = len(bits)
    current = partial
    remaining = list(range(total_bits - 1, -1, -1))
    for bit in bits:
        axis = remaining.index(bit)
        distance = 1 << bit
        route = [(i, i ^ distance) for i in range(size)]
        high = ((index >> bit) & 1) == 1
        low_part = lax.index_in_dim(current, 0, axis, keepdims=False)
        high_part = lax.index_in_dim(current, 1, axis, keepdims=False)
        keep = jnp.where(high, high_part, low_part)
        send = jnp.where(high, low_part, high_part)
        current = keep + lax.ppermute(send, "col", route)
        remaining.pop(axis)
    return current


def on_device(
    rhs,
    operator_blocks,
    local_solver,
    modes,
    coupling,
    coarse_inverse,
    send_block,
    slot_dir,
    slot_block,
):
    highest = lax.Precision.HIGHEST
    columns = rhs.shape[2]
    unknowns = rhs.shape[3]
    block_size = coupling.shape[3]
    block_count = unknowns // block_size
    mode_count = modes.shape[2]
    row_bits = lax.axis_size("row").bit_length() - 1
    col_bits = lax.axis_size("col").bit_length() - 1
    rhs_full = rhs[0, 0].astype(jnp.float32)
    operator_matrix = operator_blocks[0, 0]
    solver_matrix = local_solver[0, 0]
    mode_basis = modes[0, 0]
    couplings = coupling[0, 0]
    coarse_tile = coarse_inverse[0, :, 0, :]
    send_onehot = (send_block[0, 0][:, None] == jnp.arange(block_count)[None, :]).astype(
        jnp.bfloat16
    )
    dir_onehot = (slot_dir[0, 0][:, None] == jnp.arange(8)[None, :]).astype(jnp.bfloat16)
    block_onehot = (slot_block[0, 0][:, None] == jnp.arange(block_count)[None, :]).astype(
        jnp.float32
    )

    def coarse_solve(rounded):
        restricted = lax.dot_general(
            mode_basis, rounded, (((1,), (1,)), ((), ())), preferred_element_type=jnp.float32
        ).astype(jnp.bfloat16)
        gathered = gather_rows(restricted, list(range(row_bits - 1, -1, -1)))
        gathered = gathered.reshape(-1, columns)
        partial_sums = lax.dot_general(
            coarse_tile, gathered, (((0,), (0,)), ((), ())), preferred_element_type=jnp.float32
        )
        partial_sums = partial_sums.reshape((2,) * col_bits + (mode_count, columns))
        own_rows = scatter_cols(partial_sums, list(range(col_bits)))
        return own_rows.astype(jnp.bfloat16)

    solution = jnp.zeros((columns, unknowns), jnp.float32)
    pending = None
    for iteration in range(ITERS):
        if iteration == 0:
            residual = rhs_full
        else:
            field_half = solution.astype(jnp.bfloat16)
            blocks = field_half.reshape(columns, block_count, block_size)
            outgoing = jnp.einsum(
                "ckn,ek->ecn", blocks, send_onehot, preferred_element_type=jnp.float32
            ).astype(jnp.bfloat16)
            incoming = neighbour_pieces(outgoing)
            chosen = jnp.einsum(
                "sd,dcn->scn", dir_onehot, incoming, preferred_element_type=jnp.float32
            ).astype(jnp.bfloat16)
            coupled = jnp.einsum(
                "scn,snm->scm", chosen, couplings, preferred_element_type=jnp.float32
            )
            placed = jnp.einsum("scm,sk->ckm", coupled, block_onehot, precision=highest).reshape(
                columns, unknowns
            )
            residual = rhs_full - (
                jnp.dot(field_half, operator_matrix, preferred_element_type=jnp.float32) + placed
            )
        rounded = residual.astype(jnp.bfloat16)
        update = jnp.dot(rounded, solver_matrix, preferred_element_type=jnp.float32)
        fresh = coarse_solve(rounded) if iteration + 1 < ITERS else None
        if pending is not None:
            update = update + lax.dot_general(
                pending, mode_basis, (((0,), (0,)), ((), ())), preferred_element_type=jnp.float32
            )
        solution = solution + update
        pending = fresh
    return solution[None, None]


def solution(mesh):
    in_specs = (
        P("row", "col", None, None),
        P("row", "col", None, None),
        P("row", "col", None, None),
        P("row", "col", None, None),
        P("row", "col", None, None, None),
        P("col", None, "row", None),
        P("row", "col", None),
        P("row", "col", None),
        P("row", "col", None),
    )
    out_specs = P("row", "col", None, None)
    return jax.shard_map(
        on_device, mesh=mesh, in_specs=in_specs, out_specs=out_specs, check_vma=False
    )
```

```python
import jax
import jax.numpy as jnp
from jax import lax
from jax.sharding import PartitionSpec as P

ITERS = 6


OFFSETS = ((-1, -1), (-1, 0), (-1, 1), (0, -1), (0, 1), (1, -1), (1, 0), (1, 1))


def shifted(block, axis, distance):
    size = lax.axis_size(axis)
    route = [(i + distance, i) for i in range(size) if 0 <= i + distance < size]
    return lax.ppermute(block, axis, route)


def neighbour_pieces(outgoing):
    from_above = shifted(outgoing[jnp.array([7, 6, 5])], "row", -1)
    from_below = shifted(outgoing[jnp.array([2, 1, 0])], "row", 1)
    to_right = jnp.stack([from_above[0], outgoing[4], from_below[0]], 0)
    to_left = jnp.stack([from_above[2], outgoing[3], from_below[2]], 0)
    from_left = shifted(to_right, "col", -1)
    from_right = shifted(to_left, "col", 1)
    return jnp.stack(
        [
            from_left[0],
            from_above[1],
            from_right[0],
            from_left[1],
            from_right[1],
            from_left[2],
            from_below[1],
            from_right[2],
        ],
        0,
    )


def gather_rows(piece, bits):
    index = lax.axis_index("row")
    size = lax.axis_size("row")
    current = piece
    for step, bit in enumerate(bits):
        distance = 1 << bit
        route = [(i, i ^ distance) for i in range(size)]
        other = lax.ppermute(current, "row", route)
        high = ((index >> bit) & 1) == 1
        low_part = jnp.where(high, other, current)
        high_part = jnp.where(high, current, other)
        current = jnp.stack([low_part, high_part], axis=step)
    return current


def on_device(
    rhs,
    operator_blocks,
    local_solver,
    modes,
    coupling,
    coarse_inverse,
    send_block,
    slot_dir,
    slot_block,
):
    highest = lax.Precision.HIGHEST
    columns = rhs.shape[2]
    unknowns = rhs.shape[3]
    block_size = coupling.shape[3]
    block_count = unknowns // block_size
    mode_count = modes.shape[2]
    row_bits = lax.axis_size("row").bit_length() - 1
    rhs_full = rhs[0, 0].astype(jnp.float32)
    operator_matrix = operator_blocks[0, 0]
    solver_matrix = local_solver[0, 0]
    mode_basis = modes[0, 0]
    couplings = coupling[0, 0]
    coarse_tile = coarse_inverse[0, :, 0, :]
    send_onehot = (send_block[0, 0][:, None] == jnp.arange(block_count)[None, :]).astype(
        jnp.bfloat16
    )
    dir_onehot = (slot_dir[0, 0][:, None] == jnp.arange(8)[None, :]).astype(jnp.bfloat16)
    block_onehot = (slot_block[0, 0][:, None] == jnp.arange(block_count)[None, :]).astype(
        jnp.float32
    )

    def coarse_solve(rounded):
        restricted = lax.dot_general(
            mode_basis, rounded, (((1,), (1,)), ((), ())), preferred_element_type=jnp.float32
        ).astype(jnp.bfloat16)
        gathered = gather_rows(restricted, list(range(row_bits - 1, -1, -1)))
        gathered = gathered.reshape(-1, columns)
        partial_sums = lax.dot_general(
            coarse_tile, gathered, (((0,), (0,)), ((), ())), preferred_element_type=jnp.float32
        )
        own_rows = lax.psum_scatter(
            partial_sums.reshape(-1, 128), "col", scatter_dimension=0, tiled=True
        )
        return own_rows.reshape(mode_count, columns).astype(jnp.bfloat16)

    solution = jnp.zeros((columns, unknowns), jnp.float32)
    pending = None
    for iteration in range(ITERS):
        if iteration == 0:
            residual = rhs_full
        else:
            field_half = solution.astype(jnp.bfloat16)
            blocks = field_half.reshape(columns, block_count, block_size)
            outgoing = jnp.einsum(
                "ckn,ek->ecn", blocks, send_onehot, preferred_element_type=jnp.float32
            ).astype(jnp.bfloat16)
            incoming = neighbour_pieces(outgoing)
            chosen = jnp.einsum(
                "sd,dcn->scn", dir_onehot, incoming, preferred_element_type=jnp.float32
            ).astype(jnp.bfloat16)
            coupled = jnp.einsum(
                "scn,snm->scm", chosen, couplings, preferred_element_type=jnp.float32
            )
            placed = jnp.einsum("scm,sk->ckm", coupled, block_onehot, precision=highest).reshape(
                columns, unknowns
            )
            residual = rhs_full - (
                jnp.dot(field_half, operator_matrix, preferred_element_type=jnp.float32) + placed
            )
        rounded = residual.astype(jnp.bfloat16)
        update = jnp.dot(rounded, solver_matrix, preferred_element_type=jnp.float32)
        fresh = coarse_solve(rounded) if iteration + 1 < ITERS else None
        if pending is not None:
            update = update + lax.dot_general(
                pending, mode_basis, (((0,), (0,)), ((), ())), preferred_element_type=jnp.float32
            )
        solution = solution + update
        pending = fresh
    return solution[None, None]


def solution(mesh):
    in_specs = (
        P("row", "col", None, None),
        P("row", "col", None, None),
        P("row", "col", None, None),
        P("row", "col", None, None),
        P("row", "col", None, None, None),
        P("col", None, "row", None),
        P("row", "col", None),
        P("row", "col", None),
        P("row", "col", None),
    )
    out_specs = P("row", "col", None, None)
    return jax.shard_map(
        on_device, mesh=mesh, in_specs=in_specs, out_specs=out_specs, check_vma=False
    )
```

```python
import jax
import jax.numpy as jnp
from jax import lax
from jax.sharding import PartitionSpec as P

ITERS = 6

SEND_ORDER = (7, 6, 5, 2, 1, 0, 4, 3)
RECV_DIRS = (0, 3, 5, 2, 4, 7, 1, 6)


def shifted(block, axis, distance):
    size = lax.axis_size(axis)
    route = [(i + distance, i) for i in range(size) if 0 <= i + distance < size]
    return lax.ppermute(block, axis, route)


def neighbour_pieces(outgoing, width):
    from_above = shifted(outgoing[:, 0 : 3 * width], "row", -1)
    from_below = shifted(outgoing[:, 3 * width : 6 * width], "row", 1)
    to_right = jnp.concatenate(
        [from_above[:, :width], outgoing[:, 6 * width : 7 * width], from_below[:, :width]], 1
    )
    to_left = jnp.concatenate(
        [from_above[:, 2 * width :], outgoing[:, 7 * width :], from_below[:, 2 * width :]], 1
    )
    from_left = shifted(to_right, "col", -1)
    from_right = shifted(to_left, "col", 1)
    return jnp.concatenate(
        [from_left, from_right, from_above[:, width : 2 * width], from_below[:, width : 2 * width]],
        1,
    )


def gather_rows(piece, bits):
    index = lax.axis_index("row")
    size = lax.axis_size("row")
    current = piece
    for step, bit in enumerate(bits):
        distance = 1 << bit
        route = [(i, i ^ distance) for i in range(size)]
        other = lax.ppermute(current, "row", route)
        high = ((index >> bit) & 1) == 1
        low_part = jnp.where(high, other, current)
        high_part = jnp.where(high, current, other)
        current = jnp.stack([low_part, high_part], axis=step)
    return current


def scatter_cols(partial, bits):
    index = lax.axis_index("col")
    size = lax.axis_size("col")
    current = partial
    remaining = list(range(len(bits) - 1, -1, -1))
    for bit in bits:
        axis = remaining.index(bit)
        distance = 1 << bit
        route = [(i, i ^ distance) for i in range(size)]
        high = ((index >> bit) & 1) == 1
        low_part = lax.index_in_dim(current, 0, axis, keepdims=False)
        high_part = lax.index_in_dim(current, 1, axis, keepdims=False)
        keep = jnp.where(high, high_part, low_part)
        send = jnp.where(high, low_part, high_part)
        current = keep + lax.ppermute(send, "col", route)
        remaining.pop(axis)
    return current


def on_device(
    rhs,
    operator_blocks,
    local_solver,
    modes,
    coupling,
    coarse_inverse,
    send_block,
    slot_dir,
    slot_block,
):
    columns = rhs.shape[2]
    unknowns = rhs.shape[3]
    block_size = coupling.shape[3]
    block_count = unknowns // block_size
    mode_count = modes.shape[2]
    row_bits = lax.axis_size("row").bit_length() - 1
    col_bits = lax.axis_size("col").bit_length() - 1
    rhs_full = rhs[0, 0].astype(jnp.float32)
    solver_matrix = local_solver[0, 0]
    mode_basis = modes[0, 0]
    coarse_tile = coarse_inverse[0, :, 0, :]
    eye = jnp.eye(block_size, dtype=jnp.float32)

    send_onehot = (
        send_block[0, 0][jnp.array(SEND_ORDER)][:, None] == jnp.arange(block_count)[None, :]
    ).astype(jnp.float32)
    select = jnp.einsum("jk,nm->knjm", send_onehot, eye).reshape(unknowns, -1).astype(jnp.bfloat16)

    slot_of = (slot_dir[0, 0][:, None] == jnp.array(RECV_DIRS)[None, :]).astype(jnp.float32)
    block_of = (slot_block[0, 0][:, None] == jnp.arange(block_count)[None, :]).astype(jnp.float32)
    placed_matrix = jnp.einsum(
        "sj,sk,snm->jnkm", slot_of, block_of, coupling[0, 0].astype(jnp.float32)
    ).reshape(-1, unknowns)
    operator_matrix = jnp.concatenate(
        [operator_blocks[0, 0], placed_matrix.astype(jnp.bfloat16)], 0
    )

    def coarse_solve(rounded):
        restricted = lax.dot_general(
            mode_basis, rounded, (((1,), (1,)), ((), ())), preferred_element_type=jnp.float32
        ).astype(jnp.bfloat16)
        gathered = gather_rows(restricted, list(range(row_bits - 1, -1, -1)))
        gathered = gathered.reshape(-1, columns)
        partial_sums = lax.dot_general(
            coarse_tile, gathered, (((0,), (0,)), ((), ())), preferred_element_type=jnp.float32
        )
        partial_sums = partial_sums.reshape((2,) * col_bits + (mode_count, columns))
        own_rows = scatter_cols(partial_sums, list(range(col_bits)))
        return own_rows.astype(jnp.bfloat16)

    solution = jnp.zeros((columns, unknowns), jnp.float32)
    pending = None
    for iteration in range(ITERS):
        if iteration == 0:
            residual = rhs_full
        else:
            field_half = solution.astype(jnp.bfloat16)
            outgoing = jnp.dot(field_half, select, preferred_element_type=jnp.float32).astype(
                jnp.bfloat16
            )
            incoming = neighbour_pieces(outgoing, block_size)
            stacked = jnp.concatenate([field_half, incoming], 1)
            residual = rhs_full - jnp.dot(
                stacked, operator_matrix, preferred_element_type=jnp.float32
            )
        rounded = residual.astype(jnp.bfloat16)
        update = jnp.dot(rounded, solver_matrix, preferred_element_type=jnp.float32)
        fresh = coarse_solve(rounded) if iteration + 1 < ITERS else None
        if pending is not None:
            update = update + lax.dot_general(
                pending, mode_basis, (((0,), (0,)), ((), ())), preferred_element_type=jnp.float32
            )
        solution = solution + update
        pending = fresh
    return solution[None, None]


def solution(mesh):
    in_specs = (
        P("row", "col", None, None),
        P("row", "col", None, None),
        P("row", "col", None, None),
        P("row", "col", None, None),
        P("row", "col", None, None, None),
        P("col", None, "row", None),
        P("row", "col", None),
        P("row", "col", None),
        P("row", "col", None),
    )
    out_specs = P("row", "col", None, None)
    return jax.shard_map(
        on_device, mesh=mesh, in_specs=in_specs, out_specs=out_specs, check_vma=False
    )
```

```python
import jax
import jax.numpy as jnp
from jax import lax
from jax.sharding import PartitionSpec as P

ITERS = 6

SEND_ORDER = (7, 6, 5, 2, 1, 0, 4, 3)
RECV_DIRS = (0, 3, 5, 2, 4, 7, 1, 6)


def shifted(block, axis, distance):
    size = lax.axis_size(axis)
    route = [(i + distance, i) for i in range(size) if 0 <= i + distance < size]
    return lax.ppermute(block, axis, route)


def neighbour_pieces(outgoing, width):
    from_above = shifted(outgoing[:, 0 : 3 * width], "row", -1)
    from_below = shifted(outgoing[:, 3 * width : 6 * width], "row", 1)
    to_right = jnp.concatenate(
        [from_above[:, :width], outgoing[:, 6 * width : 7 * width], from_below[:, :width]], 1
    )
    to_left = jnp.concatenate(
        [from_above[:, 2 * width :], outgoing[:, 7 * width :], from_below[:, 2 * width :]], 1
    )
    from_left = shifted(to_right, "col", -1)
    from_right = shifted(to_left, "col", 1)
    return jnp.concatenate(
        [from_left, from_right, from_above[:, width : 2 * width], from_below[:, width : 2 * width]],
        1,
    )


def bit_reversed(bits):
    return [int(format(i, f"0{bits}b")[::-1], 2) if bits else 0 for i in range(1 << bits)]


def gather_rows(piece):
    index = lax.axis_index("row")
    size = lax.axis_size("row")
    current = piece
    for bit in range(size.bit_length() - 2, -1, -1):
        route = [(i, i ^ (1 << bit)) for i in range(size)]
        other = lax.ppermute(current, "row", route)
        high = ((index >> bit) & 1) == 1
        current = jnp.where(
            high, jnp.concatenate([other, current], 0), jnp.concatenate([current, other], 0)
        )
    return current


def scatter_cols(partial):
    index = lax.axis_index("col")
    size = lax.axis_size("col")
    current = partial
    for bit in range(size.bit_length() - 1):
        route = [(i, i ^ (1 << bit)) for i in range(size)]
        half = current.shape[0] // 2
        high = ((index >> bit) & 1) == 1
        keep = jnp.where(high, current[half:], current[:half])
        send = jnp.where(high, current[:half], current[half:])
        current = keep + lax.ppermute(send, "col", route)
    return current


def on_device(
    rhs,
    operator_blocks,
    local_solver,
    modes,
    coupling,
    coarse_inverse,
    send_block,
    slot_dir,
    slot_block,
):
    columns = rhs.shape[2]
    unknowns = rhs.shape[3]
    block_size = coupling.shape[3]
    block_count = unknowns // block_size
    mode_count = modes.shape[2]
    row_bits = lax.axis_size("row").bit_length() - 1
    col_bits = lax.axis_size("col").bit_length() - 1
    rhs_full = rhs[0, 0].astype(jnp.float32)
    solver_matrix = local_solver[0, 0]
    mode_basis = modes[0, 0]
    eye = jnp.eye(block_size, dtype=jnp.float32)

    send_onehot = (
        send_block[0, 0][jnp.array(SEND_ORDER)][:, None] == jnp.arange(block_count)[None, :]
    ).astype(jnp.float32)
    select = jnp.einsum("jk,nm->knjm", send_onehot, eye).reshape(unknowns, -1).astype(jnp.bfloat16)

    slot_of = (slot_dir[0, 0][:, None] == jnp.array(RECV_DIRS)[None, :]).astype(jnp.bfloat16)
    block_of = (slot_block[0, 0][:, None] == jnp.arange(block_count)[None, :]).astype(jnp.bfloat16)
    placed_matrix = jnp.zeros((len(RECV_DIRS), block_size, unknowns), jnp.bfloat16)
    for slot in range(coupling.shape[2]):
        spread = jnp.tile(coupling[0, 0, slot], (1, block_count)) * jnp.repeat(
            block_of[slot], block_size
        )[None, :]
        placed_matrix = placed_matrix + slot_of[slot][:, None, None] * spread[None]
    operator_matrix = jnp.concatenate(
        [operator_blocks[0, 0], placed_matrix.reshape(-1, unknowns)], 0
    )

    rows = lax.axis_size("row")
    cols = lax.axis_size("col")
    tile = coarse_inverse[0, :, 0, :].reshape(rows, mode_count, cols, mode_count)
    tile = tile[jnp.array(bit_reversed(row_bits))][:, :, jnp.array(bit_reversed(col_bits))]
    coarse_matrix = tile.reshape(rows * mode_count, cols * mode_count).T

    def coarse_solve(rounded):
        restricted = lax.dot_general(
            mode_basis, rounded, (((1,), (1,)), ((), ())), preferred_element_type=jnp.float32
        ).astype(jnp.bfloat16)
        gathered = gather_rows(restricted)
        partial_sums = jnp.dot(coarse_matrix, gathered, preferred_element_type=jnp.float32)
        return scatter_cols(partial_sums).astype(jnp.bfloat16)

    solution = jnp.zeros((columns, unknowns), jnp.float32)
    pending = None
    for iteration in range(ITERS):
        if iteration == 0:
            residual = rhs_full
        else:
            field_half = solution.astype(jnp.bfloat16)
            outgoing = jnp.dot(field_half, select, preferred_element_type=jnp.float32).astype(
                jnp.bfloat16
            )
            incoming = neighbour_pieces(outgoing, block_size)
            stacked = jnp.concatenate([field_half, incoming], 1)
            residual = rhs_full - jnp.dot(
                stacked, operator_matrix, preferred_element_type=jnp.float32
            )
        rounded = residual.astype(jnp.bfloat16)
        update = jnp.dot(rounded, solver_matrix, preferred_element_type=jnp.float32)
        fresh = coarse_solve(rounded) if iteration + 1 < ITERS else None
        if pending is not None:
            update = update + lax.dot_general(
                pending, mode_basis, (((0,), (0,)), ((), ())), preferred_element_type=jnp.float32
            )
        solution = solution + update
        pending = fresh
    return solution[None, None]


def solution(mesh):
    in_specs = (
        P("row", "col", None, None),
        P("row", "col", None, None),
        P("row", "col", None, None),
        P("row", "col", None, None),
        P("row", "col", None, None, None),
        P("col", None, "row", None),
        P("row", "col", None),
        P("row", "col", None),
        P("row", "col", None),
    )
    out_specs = P("row", "col", None, None)
    return jax.shard_map(
        on_device, mesh=mesh, in_specs=in_specs, out_specs=out_specs, check_vma=False
    )
```

```python
import jax
import jax.numpy as jnp
from jax import lax
from jax.sharding import PartitionSpec as P

ITERS = 6

SEND_ORDER = (7, 6, 5, 2, 1, 0, 4, 3)
RECV_DIRS = (0, 3, 5, 2, 4, 7, 1, 6)


def shifted(block, axis, distance):
    size = lax.axis_size(axis)
    route = [(i + distance, i) for i in range(size) if 0 <= i + distance < size]
    return lax.ppermute(block, axis, route)


def neighbour_pieces(outgoing, width):
    from_above = shifted(outgoing[:, 0 : 3 * width], "row", -1)
    from_below = shifted(outgoing[:, 3 * width : 6 * width], "row", 1)
    to_right = jnp.concatenate(
        [from_above[:, :width], outgoing[:, 6 * width : 7 * width], from_below[:, :width]], 1
    )
    to_left = jnp.concatenate(
        [from_above[:, 2 * width :], outgoing[:, 7 * width :], from_below[:, 2 * width :]], 1
    )
    from_left = shifted(to_right, "col", -1)
    from_right = shifted(to_left, "col", 1)
    return jnp.concatenate(
        [from_left, from_right, from_above[:, width : 2 * width], from_below[:, width : 2 * width]],
        1,
    )


def gather_rows(piece):
    index = lax.axis_index("row")
    size = lax.axis_size("row")
    current = piece
    for bit in range(size.bit_length() - 1):
        route = [(i, i ^ (1 << bit)) for i in range(size)]
        other = lax.ppermute(current, "row", route)
        high = ((index >> bit) & 1) == 1
        current = jnp.where(
            high, jnp.concatenate([other, current], 0), jnp.concatenate([current, other], 0)
        )
    return current


def scatter_cols(partial):
    index = lax.axis_index("col")
    size = lax.axis_size("col")
    current = partial
    for bit in range(size.bit_length() - 2, -1, -1):
        route = [(i, i ^ (1 << bit)) for i in range(size)]
        half = current.shape[0] // 2
        high = ((index >> bit) & 1) == 1
        keep = jnp.where(high, current[half:], current[:half])
        send = jnp.where(high, current[:half], current[half:])
        current = keep + lax.ppermute(send, "col", route)
    return current


def on_device(
    rhs,
    operator_blocks,
    local_solver,
    modes,
    coupling,
    coarse_inverse,
    send_block,
    slot_dir,
    slot_block,
):
    columns = rhs.shape[2]
    unknowns = rhs.shape[3]
    block_size = coupling.shape[3]
    block_count = unknowns // block_size
    mode_count = modes.shape[2]
    rhs_full = rhs[0, 0].astype(jnp.float32)
    solver_matrix = local_solver[0, 0]
    mode_basis = modes[0, 0]
    eye = jnp.eye(block_size, dtype=jnp.float32)

    send_onehot = (
        send_block[0, 0][jnp.array(SEND_ORDER)][:, None] == jnp.arange(block_count)[None, :]
    ).astype(jnp.float32)
    select = jnp.einsum("jk,nm->knjm", send_onehot, eye).reshape(unknowns, -1).astype(jnp.bfloat16)

    slot_of = (slot_dir[0, 0][:, None] == jnp.array(RECV_DIRS)[None, :]).astype(jnp.bfloat16)
    block_of = (slot_block[0, 0][:, None] == jnp.arange(block_count)[None, :]).astype(jnp.bfloat16)
    placed_matrix = jnp.zeros((len(RECV_DIRS), block_size, unknowns), jnp.bfloat16)
    for slot in range(coupling.shape[2]):
        spread = jnp.tile(coupling[0, 0, slot], (1, block_count)) * jnp.repeat(
            block_of[slot], block_size
        )[None, :]
        placed_matrix = placed_matrix + slot_of[slot][:, None, None] * spread[None]
    operator_matrix = jnp.concatenate(
        [operator_blocks[0, 0], placed_matrix.reshape(-1, unknowns)], 0
    )

    coarse_matrix = coarse_inverse[0, :, 0, :].T

    def coarse_solve(rounded):
        restricted = lax.dot_general(
            mode_basis, rounded, (((1,), (1,)), ((), ())), preferred_element_type=jnp.float32
        ).astype(jnp.bfloat16)
        gathered = gather_rows(restricted)
        partial_sums = jnp.dot(coarse_matrix, gathered, preferred_element_type=jnp.float32)
        return scatter_cols(partial_sums).astype(jnp.bfloat16)

    solution = jnp.zeros((columns, unknowns), jnp.float32)
    pending = None
    for iteration in range(ITERS):
        if iteration == 0:
            residual = rhs_full
        else:
            field_half = solution.astype(jnp.bfloat16)
            outgoing = jnp.dot(field_half, select, preferred_element_type=jnp.float32).astype(
                jnp.bfloat16
            )
            incoming = neighbour_pieces(outgoing, block_size)
            stacked = jnp.concatenate([field_half, incoming], 1)
            residual = rhs_full - jnp.dot(
                stacked, operator_matrix, preferred_element_type=jnp.float32
            )
        rounded = residual.astype(jnp.bfloat16)
        update = jnp.dot(rounded, solver_matrix, preferred_element_type=jnp.float32)
        fresh = coarse_solve(rounded) if iteration + 1 < ITERS else None
        if pending is not None:
            update = update + lax.dot_general(
                pending, mode_basis, (((0,), (0,)), ((), ())), preferred_element_type=jnp.float32
            )
        solution = solution + update
        pending = fresh
    return solution[None, None]


def solution(mesh):
    in_specs = (
        P("row", "col", None, None),
        P("row", "col", None, None),
        P("row", "col", None, None),
        P("row", "col", None, None),
        P("row", "col", None, None, None),
        P("col", None, "row", None),
        P("row", "col", None),
        P("row", "col", None),
        P("row", "col", None),
    )
    out_specs = P("row", "col", None, None)
    return jax.shard_map(
        on_device, mesh=mesh, in_specs=in_specs, out_specs=out_specs, check_vma=False
    )
```

```python
import jax
import jax.numpy as jnp
from jax import lax
from jax.sharding import PartitionSpec as P

ITERS = 6

SEND_ORDER = (7, 6, 5, 2, 1, 0, 4, 3)
RECV_DIRS = (0, 3, 5, 2, 4, 7, 1, 6)


def shifted(block, axis, distance):
    size = lax.axis_size(axis)
    route = [(i + distance, i) for i in range(size) if 0 <= i + distance < size]
    return lax.ppermute(block, axis, route)


def neighbour_pieces(outgoing, width):
    from_above = shifted(outgoing[:, 0 : 3 * width], "row", -1)
    from_below = shifted(outgoing[:, 3 * width : 6 * width], "row", 1)
    to_right = jnp.concatenate(
        [from_above[:, :width], outgoing[:, 6 * width : 7 * width], from_below[:, :width]], 1
    )
    to_left = jnp.concatenate(
        [from_above[:, 2 * width :], outgoing[:, 7 * width :], from_below[:, 2 * width :]], 1
    )
    from_left = shifted(to_right, "col", -1)
    from_right = shifted(to_left, "col", 1)
    return jnp.concatenate(
        [from_left, from_right, from_above[:, width : 2 * width], from_below[:, width : 2 * width]],
        1,
    )


def gather_rows(piece):
    index = lax.axis_index("row")
    size = lax.axis_size("row")
    current = piece
    for bit in range(size.bit_length() - 2, -1, -1):
        route = [(i, i ^ (1 << bit)) for i in range(size)]
        other = lax.ppermute(current, "row", route)
        high = ((index >> bit) & 1) == 1
        current = jnp.where(
            high, jnp.concatenate([other, current], 0), jnp.concatenate([current, other], 0)
        )
    return current


def scatter_cols(partial, block):
    index = lax.axis_index("col")
    size = lax.axis_size("col")
    current = partial
    for bit in range(size.bit_length() - 1):
        route = [(i, i ^ (1 << bit)) for i in range(size)]
        pairs = current.reshape(-1, 2, block, current.shape[1])
        low_part = pairs[:, 0].reshape(-1, current.shape[1])
        high_part = pairs[:, 1].reshape(-1, current.shape[1])
        high = ((index >> bit) & 1) == 1
        keep = jnp.where(high, high_part, low_part)
        send = jnp.where(high, low_part, high_part)
        current = keep + lax.ppermute(send, "col", route)
    return current


def on_device(
    rhs,
    operator_blocks,
    local_solver,
    modes,
    coupling,
    coarse_inverse,
    send_block,
    slot_dir,
    slot_block,
):
    columns = rhs.shape[2]
    unknowns = rhs.shape[3]
    block_size = coupling.shape[3]
    block_count = unknowns // block_size
    mode_count = modes.shape[2]
    rhs_full = rhs[0, 0].astype(jnp.float32)
    solver_matrix = local_solver[0, 0]
    mode_basis = modes[0, 0]
    eye = jnp.eye(block_size, dtype=jnp.float32)

    send_onehot = (
        send_block[0, 0][jnp.array(SEND_ORDER)][:, None] == jnp.arange(block_count)[None, :]
    ).astype(jnp.float32)
    select = jnp.einsum("jk,nm->knjm", send_onehot, eye).reshape(unknowns, -1).astype(jnp.bfloat16)

    slot_of = (slot_dir[0, 0][:, None] == jnp.array(RECV_DIRS)[None, :]).astype(jnp.bfloat16)
    block_of = (slot_block[0, 0][:, None] == jnp.arange(block_count)[None, :]).astype(jnp.bfloat16)
    placed_matrix = jnp.zeros((len(RECV_DIRS), block_size, unknowns), jnp.bfloat16)
    for slot in range(coupling.shape[2]):
        spread = jnp.tile(coupling[0, 0, slot], (1, block_count)) * jnp.repeat(
            block_of[slot], block_size
        )[None, :]
        placed_matrix = placed_matrix + slot_of[slot][:, None, None] * spread[None]
    operator_matrix = jnp.concatenate(
        [operator_blocks[0, 0], placed_matrix.reshape(-1, unknowns)], 0
    )

    rows = lax.axis_size("row")
    row_bits = rows.bit_length() - 1
    tile = coarse_inverse[0, :, 0, :].reshape((2,) * row_bits + (mode_count, -1))
    tile = jnp.transpose(tile, tuple(range(row_bits - 1, -1, -1)) + (row_bits, row_bits + 1))
    coarse_matrix = tile.reshape(rows * mode_count, -1).T

    def coarse_solve(rounded):
        restricted = lax.dot_general(
            mode_basis, rounded, (((1,), (1,)), ((), ())), preferred_element_type=jnp.float32
        ).astype(jnp.bfloat16)
        gathered = gather_rows(restricted)
        partial_sums = jnp.dot(coarse_matrix, gathered, preferred_element_type=jnp.float32)
        return scatter_cols(partial_sums, mode_count).astype(jnp.bfloat16)

    solution = jnp.zeros((columns, unknowns), jnp.float32)
    pending = None
    for iteration in range(ITERS):
        if iteration == 0:
            residual = rhs_full
        else:
            field_half = solution.astype(jnp.bfloat16)
            outgoing = jnp.dot(field_half, select, preferred_element_type=jnp.float32).astype(
                jnp.bfloat16
            )
            incoming = neighbour_pieces(outgoing, block_size)
            stacked = jnp.concatenate([field_half, incoming], 1)
            residual = rhs_full - jnp.dot(
                stacked, operator_matrix, preferred_element_type=jnp.float32
            )
        rounded = residual.astype(jnp.bfloat16)
        update = jnp.dot(rounded, solver_matrix, preferred_element_type=jnp.float32)
        fresh = coarse_solve(rounded) if iteration + 1 < ITERS else None
        if pending is not None:
            update = update + lax.dot_general(
                pending, mode_basis, (((0,), (0,)), ((), ())), preferred_element_type=jnp.float32
            )
        solution = solution + update
        pending = fresh
    return solution[None, None]


def solution(mesh):
    in_specs = (
        P("row", "col", None, None),
        P("row", "col", None, None),
        P("row", "col", None, None),
        P("row", "col", None, None),
        P("row", "col", None, None, None),
        P("col", None, "row", None),
        P("row", "col", None),
        P("row", "col", None),
        P("row", "col", None),
    )
    out_specs = P("row", "col", None, None)
    return jax.shard_map(
        on_device, mesh=mesh, in_specs=in_specs, out_specs=out_specs, check_vma=False
    )
```

```python
import jax
import numpy as np
import jax.numpy as jnp
from jax import lax
from jax.sharding import PartitionSpec as P

ITERS = 6

SEND_ORDER = (7, 6, 5, 2, 1, 0, 4, 3)
RECV_DIRS = (0, 3, 5, 2, 4, 7, 1, 6)


def shifted(block, axis, distance):
    size = lax.axis_size(axis)
    route = [(i + distance, i) for i in range(size) if 0 <= i + distance < size]
    return lax.ppermute(block, axis, route)


def neighbour_pieces(outgoing, width):
    from_above = shifted(outgoing[:, 0 : 3 * width], "row", -1)
    from_below = shifted(outgoing[:, 3 * width : 6 * width], "row", 1)
    to_right = jnp.concatenate(
        [from_above[:, :width], outgoing[:, 6 * width : 7 * width], from_below[:, :width]], 1
    )
    to_left = jnp.concatenate(
        [from_above[:, 2 * width :], outgoing[:, 7 * width :], from_below[:, 2 * width :]], 1
    )
    from_left = shifted(to_right, "col", -1)
    from_right = shifted(to_left, "col", 1)
    return jnp.concatenate(
        [from_left, from_right, from_above[:, width : 2 * width], from_below[:, width : 2 * width]],
        1,
    )


def gather_rows(piece):
    index = lax.axis_index("row")
    size = lax.axis_size("row")
    current = piece
    for bit in range(size.bit_length() - 2, -1, -1):
        route = [(i, i ^ (1 << bit)) for i in range(size)]
        other = lax.ppermute(current, "row", route)
        high = ((index >> bit) & 1) == 1
        current = jnp.where(
            high, jnp.concatenate([other, current], 0), jnp.concatenate([current, other], 0)
        )
    return current


def scatter_cols(partial):
    index = lax.axis_index("col")
    size = lax.axis_size("col")
    current = partial
    for bit in range(size.bit_length() - 1):
        route = [(i, i ^ (1 << bit)) for i in range(size)]
        half = current.shape[0] // 2
        high = ((index >> bit) & 1) == 1
        keep = jnp.where(high, current[half:], current[:half])
        send = jnp.where(high, current[:half], current[half:])
        current = keep + lax.ppermute(send, "col", route)
    return current


def reversed_blocks(count, block):
    bits = count.bit_length() - 1
    order = [int(format(i, f"0{bits}b")[::-1], 2) if bits else 0 for i in range(count)]
    return np.array([order[i // block] * block + i % block for i in range(count * block)])


def on_device(
    rhs,
    operator_blocks,
    local_solver,
    modes,
    coupling,
    coarse_inverse,
    send_block,
    slot_dir,
    slot_block,
):
    columns = rhs.shape[2]
    unknowns = rhs.shape[3]
    block_size = coupling.shape[3]
    block_count = unknowns // block_size
    mode_count = modes.shape[2]
    rhs_full = rhs[0, 0].astype(jnp.float32)
    solver_matrix = local_solver[0, 0]
    mode_basis = modes[0, 0]
    eye = jnp.eye(block_size, dtype=jnp.float32)

    send_onehot = (
        send_block[0, 0][jnp.array(SEND_ORDER)][:, None] == jnp.arange(block_count)[None, :]
    ).astype(jnp.float32)
    select = jnp.einsum("jk,nm->knjm", send_onehot, eye).reshape(unknowns, -1).astype(jnp.bfloat16)

    slot_of = (slot_dir[0, 0][:, None] == jnp.array(RECV_DIRS)[None, :]).astype(jnp.bfloat16)
    block_of = (slot_block[0, 0][:, None] == jnp.arange(block_count)[None, :]).astype(jnp.bfloat16)
    placed_matrix = jnp.zeros((len(RECV_DIRS), block_size, unknowns), jnp.bfloat16)
    for slot in range(coupling.shape[2]):
        spread = jnp.tile(coupling[0, 0, slot], (1, block_count)) * jnp.repeat(
            block_of[slot], block_size
        )[None, :]
        placed_matrix = placed_matrix + slot_of[slot][:, None, None] * spread[None]
    operator_matrix = jnp.concatenate(
        [operator_blocks[0, 0], placed_matrix.reshape(-1, unknowns)], 0
    )

    rows = lax.axis_size("row")
    cols = lax.axis_size("col")
    tile = coarse_inverse[0, :, 0, :]
    from_rows = reversed_blocks(rows, mode_count)
    from_cols = reversed_blocks(cols, mode_count)
    pick_rows = (jnp.arange(rows * mode_count)[None, :] == from_rows[:, None]).astype(jnp.bfloat16)
    pick_cols = (jnp.arange(cols * mode_count)[:, None] == from_cols[None, :]).astype(jnp.bfloat16)
    tile = jnp.dot(pick_rows, tile, preferred_element_type=jnp.float32).astype(jnp.bfloat16)
    tile = jnp.dot(tile, pick_cols, preferred_element_type=jnp.float32).astype(jnp.bfloat16)
    coarse_matrix = tile.T

    def coarse_solve(rounded):
        restricted = lax.dot_general(
            mode_basis, rounded, (((1,), (1,)), ((), ())), preferred_element_type=jnp.float32
        ).astype(jnp.bfloat16)
        gathered = gather_rows(restricted)
        partial_sums = jnp.dot(coarse_matrix, gathered, preferred_element_type=jnp.float32)
        return scatter_cols(partial_sums).astype(jnp.bfloat16)

    solution = jnp.zeros((columns, unknowns), jnp.float32)
    pending = None
    for iteration in range(ITERS):
        if iteration == 0:
            residual = rhs_full
        else:
            field_half = solution.astype(jnp.bfloat16)
            outgoing = jnp.dot(field_half, select, preferred_element_type=jnp.float32).astype(
                jnp.bfloat16
            )
            incoming = neighbour_pieces(outgoing, block_size)
            stacked = jnp.concatenate([field_half, incoming], 1)
            residual = rhs_full - jnp.dot(
                stacked, operator_matrix, preferred_element_type=jnp.float32
            )
        rounded = residual.astype(jnp.bfloat16)
        update = jnp.dot(rounded, solver_matrix, preferred_element_type=jnp.float32)
        fresh = coarse_solve(rounded) if iteration + 1 < ITERS else None
        if pending is not None:
            update = update + lax.dot_general(
                pending, mode_basis, (((0,), (0,)), ((), ())), preferred_element_type=jnp.float32
            )
        solution = solution + update
        pending = fresh
    return solution[None, None]


def solution(mesh):
    in_specs = (
        P("row", "col", None, None),
        P("row", "col", None, None),
        P("row", "col", None, None),
        P("row", "col", None, None),
        P("row", "col", None, None, None),
        P("col", None, "row", None),
        P("row", "col", None),
        P("row", "col", None),
        P("row", "col", None),
    )
    out_specs = P("row", "col", None, None)
    return jax.shard_map(
        on_device, mesh=mesh, in_specs=in_specs, out_specs=out_specs, check_vma=False
    )
```

```python
import jax
import numpy as np
import jax.numpy as jnp
from jax import lax
from jax.sharding import PartitionSpec as P

ITERS = 6

SEND_ORDER = (7, 6, 5, 2, 1, 0, 4, 3)
RECV_DIRS = (0, 3, 5, 2, 4, 7, 1, 6)


def shifted(block, axis, distance):
    size = lax.axis_size(axis)
    route = [(i + distance, i) for i in range(size) if 0 <= i + distance < size]
    return lax.ppermute(block, axis, route)


def neighbour_pieces(outgoing, width, piece):
    count = outgoing.shape[0]
    padded = jnp.pad(piece, ((0, 0), (0, 3 * width - piece.shape[1])))
    from_above = shifted(jnp.concatenate([outgoing[:, 0 : 3 * width], padded], 0), "row", -1)
    from_below = shifted(jnp.concatenate([outgoing[:, 3 * width : 6 * width], padded], 0), "row", 1)
    piece_above = from_above[count:, : piece.shape[1]]
    piece_below = from_below[count:, : piece.shape[1]]
    from_above = from_above[:count]
    from_below = from_below[:count]
    odd = (lax.axis_index("row") & 1) == 1
    pair = jnp.where(
        odd, jnp.concatenate([piece_above, piece], 0), jnp.concatenate([piece, piece_below], 0)
    )
    to_right = jnp.concatenate(
        [from_above[:, :width], outgoing[:, 6 * width : 7 * width], from_below[:, :width]], 1
    )
    to_left = jnp.concatenate(
        [from_above[:, 2 * width :], outgoing[:, 7 * width :], from_below[:, 2 * width :]], 1
    )
    from_left = shifted(to_right, "col", -1)
    from_right = shifted(to_left, "col", 1)
    incoming = jnp.concatenate(
        [from_left, from_right, from_above[:, width : 2 * width], from_below[:, width : 2 * width]],
        1,
    )
    return incoming, pair


def gather_order(size):
    bits = size.bit_length() - 1
    return [0] + list(range(bits - 1, 0, -1))


def gather_rows(pair):
    index = lax.axis_index("row")
    size = lax.axis_size("row")
    current = pair
    for bit in gather_order(size)[1:]:
        route = [(i, i ^ (1 << bit)) for i in range(size)]
        other = lax.ppermute(current, "row", route)
        high = ((index >> bit) & 1) == 1
        current = jnp.where(
            high, jnp.concatenate([other, current], 0), jnp.concatenate([current, other], 0)
        )
    return current


def scatter_cols(partial):
    index = lax.axis_index("col")
    size = lax.axis_size("col")
    current = partial
    for bit in range(size.bit_length() - 1):
        route = [(i, i ^ (1 << bit)) for i in range(size)]
        half = current.shape[0] // 2
        high = ((index >> bit) & 1) == 1
        keep = jnp.where(high, current[half:], current[:half])
        send = jnp.where(high, current[:half], current[half:])
        current = keep + lax.ppermute(send, "col", route)
    return current


def reversed_blocks(count, block, order):
    source = [sum(((i >> t) & 1) << bit for t, bit in enumerate(order)) for i in range(count)]
    return np.array([source[i // block] * block + i % block for i in range(count * block)])


def on_device(
    rhs,
    operator_blocks,
    local_solver,
    modes,
    coupling,
    coarse_inverse,
    send_block,
    slot_dir,
    slot_block,
):
    columns = rhs.shape[2]
    unknowns = rhs.shape[3]
    block_size = coupling.shape[3]
    block_count = unknowns // block_size
    mode_count = modes.shape[2]
    rhs_full = rhs[0, 0].astype(jnp.float32)
    solver_matrix = local_solver[0, 0]
    mode_basis = modes[0, 0]
    eye = jnp.eye(block_size, dtype=jnp.float32)

    send_onehot = (
        send_block[0, 0][jnp.array(SEND_ORDER)][:, None] == jnp.arange(block_count)[None, :]
    ).astype(jnp.float32)
    select = jnp.einsum("jk,nm->knjm", send_onehot, eye).reshape(unknowns, -1).astype(jnp.bfloat16)

    slot_of = (slot_dir[0, 0][:, None] == jnp.array(RECV_DIRS)[None, :]).astype(jnp.bfloat16)
    block_of = (slot_block[0, 0][:, None] == jnp.arange(block_count)[None, :]).astype(jnp.bfloat16)
    placed_matrix = jnp.zeros((len(RECV_DIRS), block_size, unknowns), jnp.bfloat16)
    for slot in range(coupling.shape[2]):
        spread = jnp.tile(coupling[0, 0, slot], (1, block_count)) * jnp.repeat(
            block_of[slot], block_size
        )[None, :]
        placed_matrix = placed_matrix + slot_of[slot][:, None, None] * spread[None]
    operator_matrix = jnp.concatenate(
        [operator_blocks[0, 0], placed_matrix.reshape(-1, unknowns)], 0
    )

    rows = lax.axis_size("row")
    cols = lax.axis_size("col")
    tile = coarse_inverse[0, :, 0, :]
    from_rows = reversed_blocks(rows, mode_count, gather_order(rows))
    from_cols = reversed_blocks(cols, mode_count, list(range(cols.bit_length() - 2, -1, -1)))
    pick_rows = (jnp.arange(rows * mode_count)[None, :] == from_rows[:, None]).astype(jnp.bfloat16)
    pick_cols = (jnp.arange(cols * mode_count)[:, None] == from_cols[None, :]).astype(jnp.bfloat16)
    tile = jnp.dot(pick_rows, tile, preferred_element_type=jnp.float32).astype(jnp.bfloat16)
    tile = jnp.dot(tile, pick_cols, preferred_element_type=jnp.float32).astype(jnp.bfloat16)
    coarse_matrix = tile.T

    def restrict(rounded):
        return lax.dot_general(
            mode_basis, rounded, (((1,), (1,)), ((), ())), preferred_element_type=jnp.float32
        ).astype(jnp.bfloat16)

    def coarse_solve(pair):
        gathered = gather_rows(pair)
        partial_sums = jnp.dot(coarse_matrix, gathered, preferred_element_type=jnp.float32)
        return scatter_cols(partial_sums).astype(jnp.bfloat16)

    solution = jnp.zeros((columns, unknowns), jnp.float32)
    carried = None
    for iteration in range(ITERS):
        coarse = None
        if iteration == 0:
            residual = rhs_full
        else:
            field_half = solution.astype(jnp.bfloat16)
            outgoing = jnp.dot(field_half, select, preferred_element_type=jnp.float32).astype(
                jnp.bfloat16
            )
            incoming, pair = neighbour_pieces(outgoing, block_size, carried)
            coarse = coarse_solve(pair)
            stacked = jnp.concatenate([field_half, incoming], 1)
            residual = rhs_full - jnp.dot(
                stacked, operator_matrix, preferred_element_type=jnp.float32
            )
        rounded = residual.astype(jnp.bfloat16)
        update = jnp.dot(rounded, solver_matrix, preferred_element_type=jnp.float32)
        if iteration + 1 < ITERS:
            carried = restrict(rounded)
        if coarse is not None:
            update = update + lax.dot_general(
                coarse, mode_basis, (((0,), (0,)), ((), ())), preferred_element_type=jnp.float32
            )
        solution = solution + update
    return solution[None, None]


def solution(mesh):
    in_specs = (
        P("row", "col", None, None),
        P("row", "col", None, None),
        P("row", "col", None, None),
        P("row", "col", None, None),
        P("row", "col", None, None, None),
        P("col", None, "row", None),
        P("row", "col", None),
        P("row", "col", None),
        P("row", "col", None),
    )
    out_specs = P("row", "col", None, None)
    return jax.shard_map(
        on_device, mesh=mesh, in_specs=in_specs, out_specs=out_specs, check_vma=False
    )
```

```python
import jax
import numpy as np
import jax.numpy as jnp
from jax import lax
from jax.sharding import PartitionSpec as P

ITERS = 6

SEND_ORDER = (7, 6, 5, 2, 1, 0, 4, 3)
RECV_DIRS = (0, 3, 5, 2, 4, 7, 1, 6)


def shifted(block, axis, distance):
    size = lax.axis_size(axis)
    route = [(i + distance, i) for i in range(size) if 0 <= i + distance < size]
    return lax.ppermute(block, axis, route)


def neighbour_pieces(outgoing, width):
    from_above = shifted(outgoing[:, 0 : 3 * width], "row", -1)
    from_below = shifted(outgoing[:, 3 * width : 6 * width], "row", 1)
    to_right = jnp.concatenate(
        [from_above[:, :width], outgoing[:, 6 * width : 7 * width], from_below[:, :width]], 1
    )
    to_left = jnp.concatenate(
        [from_above[:, 2 * width :], outgoing[:, 7 * width :], from_below[:, 2 * width :]], 1
    )
    from_left = shifted(to_right, "col", -1)
    from_right = shifted(to_left, "col", 1)
    return jnp.concatenate(
        [from_left, from_right, from_above[:, width : 2 * width], from_below[:, width : 2 * width]],
        1,
    )


def gather_rows(piece):
    index = lax.axis_index("row")
    size = lax.axis_size("row")
    current = piece
    for bit in range(size.bit_length() - 2, -1, -1):
        route = [(i, i ^ (1 << bit)) for i in range(size)]
        other = lax.ppermute(current, "row", route)
        high = ((index >> bit) & 1) == 1
        current = jnp.where(
            high, jnp.concatenate([other, current], 0), jnp.concatenate([current, other], 0)
        )
    return current


def scatter_cols(partial):
    index = lax.axis_index("col")
    size = lax.axis_size("col")
    current = partial
    for bit in range(size.bit_length() - 1):
        route = [(i, i ^ (1 << bit)) for i in range(size)]
        half = current.shape[0] // 2
        high = ((index >> bit) & 1) == 1
        keep = jnp.where(high, current[half:], current[:half])
        send = jnp.where(high, current[:half], current[half:])
        current = keep + lax.ppermute(send, "col", route)
    return current


def reversed_blocks(count, block):
    bits = count.bit_length() - 1
    order = [int(format(i, f"0{bits}b")[::-1], 2) if bits else 0 for i in range(count)]
    return np.array([order[i // block] * block + i % block for i in range(count * block)])


def on_device(
    rhs,
    operator_blocks,
    local_solver,
    modes,
    coupling,
    coarse_inverse,
    send_block,
    slot_dir,
    slot_block,
):
    columns = rhs.shape[2]
    unknowns = rhs.shape[3]
    block_size = coupling.shape[3]
    block_count = unknowns // block_size
    mode_count = modes.shape[2]
    rhs_full = rhs[0, 0].astype(jnp.float32)
    solver_matrix = local_solver[0, 0]
    mode_basis = modes[0, 0]
    eye = jnp.eye(block_size, dtype=jnp.float32)

    send_onehot = (
        send_block[0, 0][jnp.array(SEND_ORDER)][:, None] == jnp.arange(block_count)[None, :]
    ).astype(jnp.float32)
    select = jnp.einsum("jk,nm->knjm", send_onehot, eye).reshape(unknowns, -1).astype(jnp.bfloat16)

    slot_of = (slot_dir[0, 0][:, None] == jnp.array(RECV_DIRS)[None, :]).astype(jnp.bfloat16)
    block_of = (slot_block[0, 0][:, None] == jnp.arange(block_count)[None, :]).astype(jnp.bfloat16)
    placed_matrix = jnp.zeros((len(RECV_DIRS), block_size, unknowns), jnp.bfloat16)
    for slot in range(coupling.shape[2]):
        spread = jnp.tile(coupling[0, 0, slot], (1, block_count)) * jnp.repeat(
            block_of[slot], block_size
        )[None, :]
        placed_matrix = placed_matrix + slot_of[slot][:, None, None] * spread[None]
    operator_matrix = jnp.concatenate(
        [operator_blocks[0, 0], placed_matrix.reshape(-1, unknowns)], 0
    )

    rows = lax.axis_size("row")
    cols = lax.axis_size("col")
    tile = coarse_inverse[0, :, 0, :]
    from_rows = reversed_blocks(rows, mode_count)
    from_cols = reversed_blocks(cols, mode_count)
    from_row_blocks = from_rows[::mode_count] // mode_count
    pick_rows = (jnp.arange(rows)[None, :] == from_row_blocks[:, None]).astype(jnp.bfloat16)
    pick_cols = (jnp.arange(cols * mode_count)[:, None] == from_cols[None, :]).astype(jnp.bfloat16)
    tile = jnp.einsum(
        "ij,jmn->imn", pick_rows, tile.reshape(rows, mode_count, -1),
        preferred_element_type=jnp.float32,
    ).astype(jnp.bfloat16).reshape(rows * mode_count, -1)
    tile = jnp.dot(tile, pick_cols, preferred_element_type=jnp.float32).astype(jnp.bfloat16)
    coarse_matrix = tile.T

    def coarse_solve(rounded):
        restricted = lax.dot_general(
            mode_basis, rounded, (((1,), (1,)), ((), ())), preferred_element_type=jnp.float32
        ).astype(jnp.bfloat16)
        gathered = gather_rows(restricted)
        partial_sums = jnp.dot(coarse_matrix, gathered, preferred_element_type=jnp.float32)
        return scatter_cols(partial_sums).astype(jnp.bfloat16)

    solution = jnp.zeros((columns, unknowns), jnp.float32)
    pending = None
    for iteration in range(ITERS):
        if iteration == 0:
            residual = rhs_full
        else:
            field_half = solution.astype(jnp.bfloat16)
            outgoing = jnp.dot(field_half, select, preferred_element_type=jnp.float32).astype(
                jnp.bfloat16
            )
            incoming = neighbour_pieces(outgoing, block_size)
            stacked = jnp.concatenate([field_half, incoming], 1)
            residual = rhs_full - jnp.dot(
                stacked, operator_matrix, preferred_element_type=jnp.float32
            )
        rounded = residual.astype(jnp.bfloat16)
        update = jnp.dot(rounded, solver_matrix, preferred_element_type=jnp.float32)
        fresh = coarse_solve(rounded) if iteration + 1 < ITERS else None
        if pending is not None:
            update = update + lax.dot_general(
                pending, mode_basis, (((0,), (0,)), ((), ())), preferred_element_type=jnp.float32
            )
        solution = solution + update
        pending = fresh
    return solution[None, None]


def solution(mesh):
    in_specs = (
        P("row", "col", None, None),
        P("row", "col", None, None),
        P("row", "col", None, None),
        P("row", "col", None, None),
        P("row", "col", None, None, None),
        P("col", None, "row", None),
        P("row", "col", None),
        P("row", "col", None),
        P("row", "col", None),
    )
    out_specs = P("row", "col", None, None)
    return jax.shard_map(
        on_device, mesh=mesh, in_specs=in_specs, out_specs=out_specs, check_vma=False
    )
```

```python
import jax
import numpy as np
import jax.numpy as jnp
from jax import lax
from jax.sharding import PartitionSpec as P

ITERS = 6

SEND_ORDER = (7, 6, 5, 2, 1, 0, 4, 3)
RECV_DIRS = (0, 3, 5, 2, 4, 7, 1, 6)


def shifted(block, axis, distance):
    size = lax.axis_size(axis)
    route = [(i + distance, i) for i in range(size) if 0 <= i + distance < size]
    return lax.ppermute(block, axis, route)


def neighbour_pieces(outgoing, width):
    from_above = shifted(outgoing[:, 0 : 3 * width], "row", -1)
    from_below = shifted(outgoing[:, 3 * width : 6 * width], "row", 1)
    to_right = jnp.concatenate(
        [from_above[:, :width], outgoing[:, 6 * width : 7 * width], from_below[:, :width]], 1
    )
    to_left = jnp.concatenate(
        [from_above[:, 2 * width :], outgoing[:, 7 * width :], from_below[:, 2 * width :]], 1
    )
    from_left = shifted(to_right, "col", -1)
    from_right = shifted(to_left, "col", 1)
    return jnp.concatenate(
        [from_left, from_right, from_above[:, width : 2 * width], from_below[:, width : 2 * width]],
        1,
    )


def gather_rows(piece):
    index = lax.axis_index("row")
    size = lax.axis_size("row")
    current = piece
    for bit in range(size.bit_length() - 2, -1, -1):
        route = [(i, i ^ (1 << bit)) for i in range(size)]
        other = lax.ppermute(current, "row", route)
        high = ((index >> bit) & 1) == 1
        current = jnp.where(
            high, jnp.concatenate([other, current], 0), jnp.concatenate([current, other], 0)
        )
    return current


def scatter_cols(partial):
    index = lax.axis_index("col")
    size = lax.axis_size("col")
    current = partial
    for bit in range(size.bit_length() - 1):
        route = [(i, i ^ (1 << bit)) for i in range(size)]
        half = current.shape[0] // 2
        high = ((index >> bit) & 1) == 1
        keep = jnp.where(high, current[half:], current[:half])
        send = jnp.where(high, current[:half], current[half:])
        received = lax.ppermute(send.astype(jnp.bfloat16), "col", route)
        current = keep + received.astype(jnp.float32)
    return current


def reversed_blocks(count, block):
    bits = count.bit_length() - 1
    order = [int(format(i, f"0{bits}b")[::-1], 2) if bits else 0 for i in range(count)]
    return np.array([order[i // block] * block + i % block for i in range(count * block)])


def on_device(
    rhs,
    operator_blocks,
    local_solver,
    modes,
    coupling,
    coarse_inverse,
    send_block,
    slot_dir,
    slot_block,
):
    columns = rhs.shape[2]
    unknowns = rhs.shape[3]
    block_size = coupling.shape[3]
    block_count = unknowns // block_size
    mode_count = modes.shape[2]
    rhs_full = rhs[0, 0].astype(jnp.float32)
    solver_matrix = local_solver[0, 0]
    mode_basis = modes[0, 0]
    eye = jnp.eye(block_size, dtype=jnp.float32)

    send_onehot = (
        send_block[0, 0][jnp.array(SEND_ORDER)][:, None] == jnp.arange(block_count)[None, :]
    ).astype(jnp.float32)
    select = jnp.einsum("jk,nm->knjm", send_onehot, eye).reshape(unknowns, -1).astype(jnp.bfloat16)

    slot_of = (slot_dir[0, 0][:, None] == jnp.array(RECV_DIRS)[None, :]).astype(jnp.bfloat16)
    block_of = (slot_block[0, 0][:, None] == jnp.arange(block_count)[None, :]).astype(jnp.bfloat16)
    placed_matrix = jnp.zeros((len(RECV_DIRS), block_size, unknowns), jnp.bfloat16)
    for slot in range(coupling.shape[2]):
        spread = jnp.tile(coupling[0, 0, slot], (1, block_count)) * jnp.repeat(
            block_of[slot], block_size
        )[None, :]
        placed_matrix = placed_matrix + slot_of[slot][:, None, None] * spread[None]
    operator_matrix = jnp.concatenate(
        [operator_blocks[0, 0], placed_matrix.reshape(-1, unknowns)], 0
    )

    rows = lax.axis_size("row")
    cols = lax.axis_size("col")
    tile = coarse_inverse[0, :, 0, :]
    from_rows = reversed_blocks(rows, mode_count)
    from_cols = reversed_blocks(cols, mode_count)
    pick_rows = (jnp.arange(rows * mode_count)[None, :] == from_rows[:, None]).astype(jnp.bfloat16)
    pick_cols = (jnp.arange(cols * mode_count)[:, None] == from_cols[None, :]).astype(jnp.bfloat16)
    tile = jnp.dot(pick_rows, tile, preferred_element_type=jnp.float32).astype(jnp.bfloat16)
    tile = jnp.dot(tile, pick_cols, preferred_element_type=jnp.float32).astype(jnp.bfloat16)
    coarse_matrix = tile.T

    def coarse_solve(rounded):
        restricted = lax.dot_general(
            mode_basis, rounded, (((1,), (1,)), ((), ())), preferred_element_type=jnp.float32
        ).astype(jnp.bfloat16)
        gathered = gather_rows(restricted)
        partial_sums = jnp.dot(coarse_matrix, gathered, preferred_element_type=jnp.float32)
        return scatter_cols(partial_sums).astype(jnp.bfloat16)

    solution = jnp.zeros((columns, unknowns), jnp.float32)
    pending = None
    for iteration in range(ITERS):
        if iteration == 0:
            residual = rhs_full
        else:
            field_half = solution.astype(jnp.bfloat16)
            outgoing = jnp.dot(field_half, select, preferred_element_type=jnp.float32).astype(
                jnp.bfloat16
            )
            incoming = neighbour_pieces(outgoing, block_size)
            stacked = jnp.concatenate([field_half, incoming], 1)
            residual = rhs_full - jnp.dot(
                stacked, operator_matrix, preferred_element_type=jnp.float32
            )
        rounded = residual.astype(jnp.bfloat16)
        update = jnp.dot(rounded, solver_matrix, preferred_element_type=jnp.float32)
        fresh = coarse_solve(rounded) if iteration + 1 < ITERS else None
        if pending is not None:
            update = update + lax.dot_general(
                pending, mode_basis, (((0,), (0,)), ((), ())), preferred_element_type=jnp.float32
            )
        solution = solution + update
        pending = fresh
    return solution[None, None]


def solution(mesh):
    in_specs = (
        P("row", "col", None, None),
        P("row", "col", None, None),
        P("row", "col", None, None),
        P("row", "col", None, None),
        P("row", "col", None, None, None),
        P("col", None, "row", None),
        P("row", "col", None),
        P("row", "col", None),
        P("row", "col", None),
    )
    out_specs = P("row", "col", None, None)
    return jax.shard_map(
        on_device, mesh=mesh, in_specs=in_specs, out_specs=out_specs, check_vma=False
    )
```
